128 devices in a mesh: feat: 8 (over y, core), dom: 16 (over z, x).
Axes of the slice: x: 4, y: 4, z: 4, core: 2. Of those that a mesh axis runs over, the one named last changes fastest.
Arguments:
- features: bfloat16 [768, 262144], P('feat', 'dom'), may hold values from -6 to 6
- neighbours: int32 [65536, 15], P('dom'), may hold values from 0 to 16383
- self_first: bfloat16 [768, 1024], replicated, may hold values from -0.21875 to 0.21875
- neighbour_first: bfloat16 [768, 1024], replicated, may hold values from -0.21875 to 0.21875
- owners: int32 [655360, 1], P(('feat', 'dom')), may hold values from 0 to 15; in each aligned block of 5120 rows (0 to 5119, 5120 to 10239, ...) at most 400 rows name the same one
- offsets: int32 [65536, 10], P(('feat', 'dom')), may hold values from 0 to 511
- self_second: bfloat16 [1024, 1024], replicated, may hold values from -0.1875 to 0.1875
- neighbour_second: bfloat16 [1024, 1024], replicated, may hold values from -0.1875 to 0.1875
- cotangent: bfloat16 [65536, 1024], P(('feat', 'dom')), may hold values from -0.0234375 to 0.0234375
Outputs:
- second_out: bfloat16 [65536, 1024], P(('feat', 'dom'))
- grad_self_second: float32 [1024, 1024], replicated
- grad_neighbour_second: float32 [1024, 1024], replicated
The draws below stay inside these ranges and needn't reach their ends.
Inputs may be any that keep to these rules, and one draw needn't show every extreme that they name: `owners`: among the 5120 slots of one device (rows of one device), no partition is named more than 400 times, a bound that some block reaches.
All inputs are finite; a program needn't handle non-finite values.
Results may differ from the reference program's by a relative error of at most 0.007.
Values may be sent and summed in bfloat16 or wider, within the bound.
No kernel may reach another device: no remote copies, remote signals or barrier semaphores. Data moves between devices by JAX's collectives and lax.ppermute only.
A program may use at most 192 MiB of HBM per device.

```python
import math
import jax
import jax.numpy as jnp
import numpy as np
from jax import lax

F = 768
H = 1024
K1 = 15
K2 = 10
SRC_DEV = 16384
T1_DEV = 512
S_DEV = 512
SRC = 262144
T1_ROWS = 65536
SEEDS = 65536
SLOTS = 655360
MOST = 400
N_FEAT = 8
N_DOM = 16


def plant(result, own_key, smallest, high):
    shape = result.shape
    index_at = [jax.random.randint(jax.random.fold_in(own_key, axis), (), 0, shape[axis]) for axis in range(len(shape))]
    result = result.at[tuple(index_at)].set(smallest)
    longest = shape.index(max(shape))
    index_at[longest] = (index_at[longest] + 1) % shape[longest]
    return result.at[tuple(index_at)].set(high)


def steps_of(stream_key, dims, cuts, least, top_value):
    def one(axis_at, blocks):
        heights = jax.random.uniform(jax.random.fold_in(jax.random.fold_in(stream_key, 6), axis_at), (blocks,), jnp.float32, least / len(cuts), top_value / len(cuts))
        return jnp.repeat(jnp.exp(heights), dims[axis_at] // blocks).reshape((-1,) + (1,) * (len(dims) - axis_at - 1))

    gain = one(*cuts[0])
    for cut in cuts[1:]:
        gain = gain * one(*cut)
    return gain


def assign_block(own_key, own, number, rows, number_of, top, most, skew):
    ranking = jax.random.permutation(own_key, number_of)
    heavy_load, ordinary = shares(number_of, rows * top, most, skew, True), shares(number_of, rows * top, most, skew, False)
    places = jnp.arange(number_of)

    def named(lengths, rotation):
        used = int((lengths > 0).sum())
        fixed = max(1, used // 4)
        moved = fixed + (places - fixed + rotation * (used - fixed)) % max(1, number_of - fixed)
        return jnp.zeros((number_of,), jnp.int32).at[ranking[jnp.where(places < fixed, places, moved)]].set(jnp.asarray(lengths, jnp.int32))

    lengths = jnp.where(number % 4 == 0, named(heavy_load, number // 4), named(ordinary, number - number // 4 - 1))
    mixed = jax.random.permutation(jax.random.fold_in(own, 3), number_of)
    source_of, taker = mixed[0:number_of // 2 * 2:2], mixed[1:number_of // 2 * 2:2]
    slack = jnp.minimum(lengths[source_of] - 1, most - lengths[taker]) // 2
    slack = jnp.where((source_of == ranking[0]) | (taker == ranking[0]) | (lengths[taker] == 0), 0, jnp.maximum(slack, 0))
    moved = jax.random.randint(jax.random.fold_in(own, 4), (number_of // 2,), 0, 1 << 20) % (slack + 1)
    lengths = lengths.at[source_of].add(-moved).at[taker].add(moved)
    members = jnp.searchsorted(jnp.cumsum(lengths), jnp.arange(rows * top), side="right").astype(jnp.int32)
    grid = members.reshape(top, rows).T
    grid = grid[jax.random.permutation(jax.random.fold_in(own, 1), rows)]
    rotation = jax.random.randint(jax.random.fold_in(own, 2), (rows, 1), 0, top)
    return jnp.take_along_axis(grid, (jnp.arange(top)[None, :] + rotation) % top, axis=1)


def shares(amount, total, bound, lean, full):
    weights = [(1 << 20) // math.isqrt(grade ** lean) + 1 for grade in range(1, amount + 1)]
    largest = bound if full else min(bound, max(-(-total // amount), total * weights[0] // sum(weights)))
    least = 1 if total - largest >= amount - 1 else 0
    given, spare = [largest] + [least] * (amount - 1), total - largest - least * (amount - 1)
    while spare > 0:
        candidates = [i for i in range(1, amount) if given[i] < largest] or [i for i in range(1, amount) if given[i] < bound]
        whole, remaining = sum([weights[i] for i in candidates]), spare
        for i in candidates:
            extra = min(bound - given[i], max(1, remaining * weights[i] // whole), spare)
            given[i] = given[i] + extra
            spare = spare - extra
    return np.array(given)


def scatter_about(rng, dims, scale, reach, shards=(), kind=jnp.bfloat16):
    gain = steps_of(rng, dims, shards, -0.22, 0.18) if shards else 1.0
    array = jax.random.normal(rng, dims, jnp.float32) * scale * gain
    return jnp.minimum(jnp.maximum(array, -reach), reach).astype(kind)


def setup_inputs(seed: int = 0) -> dict:
    arg_keys = jax.random.split(jax.random.key(seed), 10)
    features = scatter_about(arg_keys[0], (F, SRC), 1.0, 6.0, ((0, 8), (1, 16)))
    neighbours = plant(jax.random.randint(arg_keys[1], (T1_ROWS, K1), 0, SRC_DEV), jax.random.fold_in(arg_keys[1], 1), 0, SRC_DEV - 1).astype(jnp.int32)
    self_first = scatter_about(arg_keys[2], (F, H), F ** -0.5, 0.21875)
    neighbour_first = scatter_about(arg_keys[3], (F, H), F ** -0.5, 0.21875)
    owners_keys = jax.random.split(jax.random.fold_in(arg_keys[4], 1), SLOTS // (S_DEV * K2))
    owners_turns = jax.random.permutation(jax.random.fold_in(arg_keys[4], 3), SLOTS // (S_DEV * K2))
    owners = jax.vmap(lambda own, number: assign_block(jax.random.fold_in(arg_keys[4], 2), own, number, S_DEV * K2, N_DOM, 1, MOST, 1))(owners_keys, owners_turns).reshape((SLOTS, 1))
    offsets = plant(jax.random.randint(arg_keys[5], (SEEDS, K2), 0, T1_DEV), jax.random.fold_in(arg_keys[5], 1), 0, T1_DEV - 1).astype(jnp.int32)
    self_second = scatter_about(arg_keys[6], (H, H), H ** -0.5, 0.1875)
    neighbour_second = scatter_about(arg_keys[7], (H, H), H ** -0.5, 0.1875)
    cotangent = scatter_about(arg_keys[8], (SEEDS, H), SEEDS ** -0.5, 0.0234375, ((0, 128),))
    return {"features": features, "neighbours": neighbours, "self_first": self_first, "neighbour_first": neighbour_first, "owners": owners, "offsets": offsets, "self_second": self_second, "neighbour_second": neighbour_second, "cotangent": cotangent}


def contract(left, right):
    return lax.dot_general(left, right, (((0,), (0,)), ((), ())), preferred_element_type=jnp.float32)


def reference(features, neighbours, self_first, neighbour_first, owners, offsets, self_second, neighbour_second, cotangent):
    targets_part = T1_DEV * N_FEAT
    layer_rows = []
    for part_index in range(N_DOM):
        block_cols = features[:, part_index * SRC_DEV:(part_index + 1) * SRC_DEV]
        lists = neighbours[part_index * targets_part:(part_index + 1) * targets_part]
        mixed_rows = (jnp.sum(block_cols[:, lists].astype(jnp.float32), axis=2) / K1).astype(jnp.bfloat16)
        own_rows = block_cols[:, :targets_part]
        pre_first = contract(own_rows, self_first) + contract(mixed_rows, neighbour_first)
        layer_rows.append(jnp.maximum(pre_first, 0.0).astype(jnp.bfloat16))
    hidden_all = jnp.stack(layer_rows)
    grouped = jnp.transpose(hidden_all.reshape(N_DOM, N_FEAT, T1_DEV, H), (1, 0, 2, 3))
    own_second = grouped[:, :, :S_DEV].reshape(N_FEAT * N_DOM * S_DEV, H)
    table = grouped.reshape(N_FEAT * N_DOM * T1_DEV, H)
    seed_count = N_FEAT * N_DOM * S_DEV
    replica = (jnp.arange(seed_count) // (S_DEV * N_DOM)).astype(jnp.int32)
    slot_owner = owners.reshape(seed_count, K2)
    running = jnp.zeros((seed_count, H), jnp.float32)
    for slot in range(K2):
        index_rows = replica * (N_DOM * T1_DEV) + slot_owner[:, slot] * T1_DEV + offsets[:, slot]
        running = running + table[index_rows].astype(jnp.float32)
    mean_second = (running / K2).astype(jnp.bfloat16)
    second_out = (jnp.dot(own_second, self_second, preferred_element_type=jnp.float32)
                  + jnp.dot(mean_second, neighbour_second, preferred_element_type=jnp.float32)).astype(jnp.bfloat16)
    grad_self = contract(own_second, cotangent)
    grad_neighbour = contract(mean_second, cotangent)
    return second_out, grad_self, grad_neighbour
```

```python
import jax
import jax.numpy as jnp
from jax import lax
from jax.sharding import PartitionSpec as P


def contract(left, right):
    return lax.dot_general(
        left, right, (((0,), (0,)), ((), ())), preferred_element_type=jnp.float32
    )


def shards(
    features,
    neighbours,
    self_first,
    neighbour_first,
    owners,
    offsets,
    self_second,
    neighbour_second,
    cotangent,
):
    columns_here = features.shape[0]
    targets_part = neighbours.shape[0]
    fanout_first = neighbours.shape[1]
    hidden_width = self_first.shape[1]
    feat_size = lax.axis_size("feat")
    share_rows = targets_part // feat_size
    node_rows = features.T
    gathered = jnp.take(node_rows, neighbours.reshape(-1), axis=0, mode="clip")
    mixed_rows = (
        jnp.sum(
            gathered.reshape(targets_part, fanout_first, columns_here),
            axis=1,
            dtype=jnp.float32,
        )
        / fanout_first
    ).astype(jnp.bfloat16)
    own_rows = node_rows[:targets_part]
    both = jnp.stack([own_rows, mixed_rows], axis=1).reshape(
        feat_size, share_rows, 2, columns_here
    )
    arrived = lax.all_to_all(both, "feat", 0, 0, tiled=True)
    lhs = jnp.transpose(arrived, (1, 0, 2, 3)).reshape(share_rows, -1)
    weights = jnp.stack(
        [
            self_first.reshape(feat_size, columns_here, hidden_width),
            neighbour_first.reshape(feat_size, columns_here, hidden_width),
        ],
        axis=1,
    ).reshape(-1, hidden_width)
    pre_first = jnp.dot(lhs, weights, preferred_element_type=jnp.float32)
    layer_out = jnp.maximum(pre_first, 0.0).astype(jnp.bfloat16)
    seed_rows = cotangent.shape[0]
    fanout_second = offsets.shape[1]
    segment = lax.all_gather(layer_out, "dom", axis=0, tiled=True)
    flat_rows = owners.reshape(seed_rows, fanout_second) * share_rows + offsets
    fetched = jnp.take(segment, flat_rows.reshape(-1), axis=0, mode="clip")
    summed = jnp.sum(
        fetched.reshape(seed_rows, fanout_second, hidden_width), axis=1, dtype=jnp.float32
    )
    mean_second = (summed / fanout_second).astype(jnp.bfloat16)
    second_out = (
        jnp.dot(layer_out, self_second, preferred_element_type=jnp.float32)
        + jnp.dot(mean_second, neighbour_second, preferred_element_type=jnp.float32)
    ).astype(jnp.bfloat16)
    grad_self = contract(layer_out, cotangent)
    grad_neighbour = contract(mean_second, cotangent)
    grad_self, grad_neighbour = lax.psum((grad_self, grad_neighbour), ("feat", "dom"))
    return (second_out, grad_self, grad_neighbour)


def solution(mesh):
    placed = (
        P("feat", "dom"),
        P("dom", None),
        P(),
        P(),
        P(("feat", "dom"), None),
        P(("feat", "dom"), None),
        P(),
        P(),
        P(("feat", "dom"), None),
    )
    return jax.shard_map(
        shards,
        mesh=mesh,
        in_specs=placed,
        out_specs=(P(("feat", "dom"), None), P(), P()),
        check_vma=False,
    )
```

```python
import jax
import jax.numpy as jnp
from jax import lax
from jax.experimental import pallas as pl
from jax.experimental.pallas import tpu as pltpu
from jax.sharding import PartitionSpec as P


def contract(left, right):
    return lax.dot_general(
        left, right, (((0,), (0,)), ((), ())), preferred_element_type=jnp.float32
    )


def gather_sum(table, index, block=512, unroll=8):
    count, fanout = index.shape
    rows, width = table.shape

    def kernel(index_ref, table_ref, out_ref):
        step = pl.program_id(0)

        def body(t, carry):
            base = (step * block + t) * fanout
            acc = table_ref[pl.ds(index_ref[base], 1), :]
            for k in range(1, fanout):
                acc = acc + table_ref[pl.ds(index_ref[base + k], 1), :]
            out_ref[pl.ds(t, 1), :] = acc
            return carry

        lax.fori_loop(0, block, body, 0, unroll=unroll)

    return pl.pallas_call(
        kernel,
        out_shape=jax.ShapeDtypeStruct((count, width), jnp.float32),
        grid_spec=pltpu.PrefetchScalarGridSpec(
            num_scalar_prefetch=1,
            grid=(count // block,),
            in_specs=[pl.BlockSpec((rows, width), lambda b, i: (0, 0))],
            out_specs=pl.BlockSpec((block, width), lambda b, i: (b, 0)),
        ),
    )(index.reshape(-1), table)


def shards(
    features,
    neighbours,
    self_first,
    neighbour_first,
    owners,
    offsets,
    self_second,
    neighbour_second,
    cotangent,
):
    columns_here = features.shape[0]
    targets_part = neighbours.shape[0]
    fanout_first = neighbours.shape[1]
    hidden_width = self_first.shape[1]
    feat_size = lax.axis_size("feat")
    share_rows = targets_part // feat_size
    node_rows = features.T
    mixed_rows = (
        gather_sum(node_rows.astype(jnp.float32), neighbours) / fanout_first
    ).astype(jnp.bfloat16)
    own_rows = node_rows[:targets_part]
    both = jnp.stack([own_rows, mixed_rows], axis=1).reshape(
        feat_size, share_rows, 2, columns_here
    )
    arrived = lax.all_to_all(both, "feat", 0, 0, tiled=True)
    lhs = jnp.transpose(arrived, (1, 0, 2, 3)).reshape(share_rows, -1)
    weights = jnp.stack(
        [
            self_first.reshape(feat_size, columns_here, hidden_width),
            neighbour_first.reshape(feat_size, columns_here, hidden_width),
        ],
        axis=1,
    ).reshape(-1, hidden_width)
    pre_first = jnp.dot(lhs, weights, preferred_element_type=jnp.float32)
    layer_out = jnp.maximum(pre_first, 0.0).astype(jnp.bfloat16)
    seed_rows = cotangent.shape[0]
    fanout_second = offsets.shape[1]
    segment = lax.all_gather(layer_out, "dom", axis=0, tiled=True)
    flat_rows = owners.reshape(seed_rows, fanout_second) * share_rows + offsets
    table_index = jnp.arange(segment.shape[0], dtype=jnp.int32)[None, :]
    counts = sum(
        (flat_rows[:, k : k + 1] == table_index).astype(jnp.bfloat16)
        for k in range(fanout_second)
    )
    summed = jnp.dot(counts, segment, preferred_element_type=jnp.float32)
    mean_second = (summed / fanout_second).astype(jnp.bfloat16)
    second_out = (
        jnp.dot(layer_out, self_second, preferred_element_type=jnp.float32)
        + jnp.dot(mean_second, neighbour_second, preferred_element_type=jnp.float32)
    ).astype(jnp.bfloat16)
    grad_self = contract(layer_out, cotangent)
    grad_neighbour = contract(mean_second, cotangent)
    grad_self, grad_neighbour = lax.psum((grad_self, grad_neighbour), ("feat", "dom"))
    return (second_out, grad_self, grad_neighbour)


def solution(mesh):
    placed = (
        P("feat", "dom"),
        P("dom", None),
        P(),
        P(),
        P(("feat", "dom"), None),
        P(("feat", "dom"), None),
        P(),
        P(),
        P(("feat", "dom"), None),
    )
    return jax.shard_map(
        shards,
        mesh=mesh,
        in_specs=placed,
        out_specs=(P(("feat", "dom"), None), P(), P()),
        check_vma=False,
    )
```

```python
import jax
import jax.numpy as jnp
from jax import lax
from jax.experimental import pallas as pl
from jax.experimental.pallas import tpu as pltpu
from jax.sharding import PartitionSpec as P


def contract(left, right):
    return lax.dot_general(
        left, right, (((0,), (0,)), ((), ())), preferred_element_type=jnp.float32
    )


def gather_sum(table, index, block=512, unroll=8):
    fanout, count = index.shape
    rows, width = table.shape

    def kernel(index_ref, table_ref, out_ref):
        step = pl.program_id(0)

        def body(t, carry):
            base = step * block + t
            acc = table_ref[pl.ds(index_ref[base], 1), :]
            for k in range(1, fanout):
                acc = acc + table_ref[pl.ds(index_ref[k * count + base], 1), :]
            out_ref[pl.ds(t, 1), :] = acc
            return carry

        lax.fori_loop(0, block, body, 0, unroll=unroll)

    return pl.pallas_call(
        kernel,
        out_shape=jax.ShapeDtypeStruct((count, width), jnp.float32),
        grid_spec=pltpu.PrefetchScalarGridSpec(
            num_scalar_prefetch=1,
            grid=(count // block,),
            in_specs=[pl.BlockSpec((rows, width), lambda b, i: (0, 0))],
            out_specs=pl.BlockSpec((block, width), lambda b, i: (b, 0)),
        ),
    )(index.reshape(-1), table)


def shards(
    features,
    neighbours,
    self_first,
    neighbour_first,
    owners,
    offsets,
    self_second,
    neighbour_second,
    cotangent,
):
    columns_here = features.shape[0]
    targets_part = neighbours.shape[0]
    fanout_first = neighbours.shape[1]
    hidden_width = self_first.shape[1]
    feat_size = lax.axis_size("feat")
    share_rows = targets_part // feat_size
    mixed_rows = (
        gather_sum(features.astype(jnp.float32).T, neighbours.T) / fanout_first
    ).astype(jnp.bfloat16)
    own_rows = features[:, :targets_part].T
    both = jnp.stack([own_rows, mixed_rows], axis=1).reshape(
        feat_size, share_rows, 2, columns_here
    )
    arrived = lax.all_to_all(both, "feat", 0, 0, tiled=True)
    lhs = jnp.transpose(arrived, (1, 0, 2, 3)).reshape(share_rows, -1)
    weights = jnp.stack(
        [
            self_first.reshape(feat_size, columns_here, hidden_width),
            neighbour_first.reshape(feat_size, columns_here, hidden_width),
        ],
        axis=1,
    ).reshape(-1, hidden_width)
    pre_first = jnp.dot(lhs, weights, preferred_element_type=jnp.float32)
    layer_out = jnp.maximum(pre_first, 0.0).astype(jnp.bfloat16)
    seed_rows = cotangent.shape[0]
    fanout_second = offsets.shape[1]
    segment = lax.all_gather(layer_out, "dom", axis=0, tiled=True)
    flat_rows = owners.reshape(seed_rows, fanout_second) * share_rows + offsets
    table_index = jnp.arange(segment.shape[0], dtype=jnp.int32)[None, :]
    counts = sum(
        (flat_rows[:, k : k + 1] == table_index).astype(jnp.bfloat16)
        for k in range(fanout_second)
    )
    counts = lax.optimization_barrier(counts)
    summed = jnp.dot(counts, segment, preferred_element_type=jnp.float32)
    mean_second = (summed / fanout_second).astype(jnp.bfloat16)
    second_out = (
        jnp.dot(layer_out, self_second, preferred_element_type=jnp.float32)
        + jnp.dot(mean_second, neighbour_second, preferred_element_type=jnp.float32)
    ).astype(jnp.bfloat16)
    grad_self = contract(layer_out, cotangent)
    grad_neighbour = contract(mean_second, cotangent)
    grad_self, grad_neighbour = lax.psum((grad_self, grad_neighbour), ("feat", "dom"))
    return (second_out, grad_self, grad_neighbour)


def solution(mesh):
    placed = (
        P("feat", "dom"),
        P("dom", None),
        P(),
        P(),
        P(("feat", "dom"), None),
        P(("feat", "dom"), None),
        P(),
        P(),
        P(("feat", "dom"), None),
    )
    return jax.shard_map(
        shards,
        mesh=mesh,
        in_specs=placed,
        out_specs=(P(("feat", "dom"), None), P(), P()),
        check_vma=False,
    )
```

```python
import jax
import jax.numpy as jnp
from jax import lax
from jax.experimental import pallas as pl
from jax.experimental.pallas import tpu as pltpu
from jax.sharding import PartitionSpec as P


def contract(left, right):
    return lax.dot_general(
        left, right, (((0,), (0,)), ((), ())), preferred_element_type=jnp.float32
    )


def gather_sum(table, index, block=512, unroll=8):
    fanout, count = index.shape
    rows, width = table.shape

    def kernel(index_ref, table_ref, out_ref):
        step = pl.program_id(0)

        def body(t, carry):
            base = step * block + t
            acc = table_ref[pl.ds(index_ref[base], 1), :]
            for k in range(1, fanout):
                acc = acc + table_ref[pl.ds(index_ref[k * count + base], 1), :]
            out_ref[pl.ds(t, 1), :] = acc
            return carry

        lax.fori_loop(0, block, body, 0, unroll=unroll)

    return pl.pallas_call(
        kernel,
        out_shape=jax.ShapeDtypeStruct((count, width), jnp.float32),
        grid_spec=pltpu.PrefetchScalarGridSpec(
            num_scalar_prefetch=1,
            grid=(count // block,),
            in_specs=[pl.BlockSpec((rows, width), lambda b, i: (0, 0))],
            out_specs=pl.BlockSpec((block, width), lambda b, i: (b, 0)),
        ),
    )(index.reshape(-1), table)


def shards(
    features,
    neighbours,
    self_first,
    neighbour_first,
    owners,
    offsets,
    self_second,
    neighbour_second,
    cotangent,
):
    columns_here = features.shape[0]
    targets_part = neighbours.shape[0]
    fanout_first = neighbours.shape[1]
    hidden_width = self_first.shape[1]
    feat_size = lax.axis_size("feat")
    share_rows = targets_part // feat_size
    pieces = 2
    piece_rows = share_rows // pieces
    weights = jnp.stack(
        [
            self_first.reshape(feat_size, columns_here, hidden_width),
            neighbour_first.reshape(feat_size, columns_here, hidden_width),
        ],
        axis=1,
    ).reshape(-1, hidden_width)
    table = features.astype(jnp.float32).T
    lists = neighbours.T.reshape(fanout_first, feat_size, share_rows)
    own_all = features[:, :targets_part].reshape(columns_here, feat_size, share_rows)
    seed_rows = cotangent.shape[0]
    fanout_second = offsets.shape[1]
    slot_owner = owners.reshape(seed_rows, fanout_second)
    layer_parts = []
    summed = None
    for c in range(pieces):
        rows = slice(c * piece_rows, (c + 1) * piece_rows)
        mixed_rows = (
            gather_sum(table, lists[:, :, rows].reshape(fanout_first, -1)) / fanout_first
        ).astype(jnp.bfloat16)
        own_rows = jnp.transpose(own_all[:, :, rows], (1, 2, 0))
        both = jnp.stack(
            [own_rows, mixed_rows.reshape(feat_size, piece_rows, columns_here)], axis=2
        )
        arrived = lax.all_to_all(both, "feat", 0, 0, tiled=True)
        lhs = jnp.transpose(arrived, (1, 0, 2, 3)).reshape(piece_rows, -1)
        pre_first = jnp.dot(lhs, weights, preferred_element_type=jnp.float32)
        part_out = jnp.maximum(pre_first, 0.0).astype(jnp.bfloat16)
        layer_parts.append(part_out)
        segment = lax.all_gather(part_out, "dom", axis=0, tiled=True)
        inside = offsets // piece_rows == c
        flat_rows = jnp.where(inside, slot_owner * piece_rows + offsets - c * piece_rows, -1)
        table_index = jnp.arange(segment.shape[0], dtype=jnp.int32)[None, :]
        counts = sum(
            (flat_rows[:, k : k + 1] == table_index).astype(jnp.bfloat16)
            for k in range(fanout_second)
        )
        counts = lax.optimization_barrier(counts)
        term = jnp.dot(counts, segment, preferred_element_type=jnp.float32)
        summed = term if summed is None else summed + term
    layer_out = jnp.concatenate(layer_parts, axis=0)
    mean_second = (summed / fanout_second).astype(jnp.bfloat16)
    second_out = (
        jnp.dot(layer_out, self_second, preferred_element_type=jnp.float32)
        + jnp.dot(mean_second, neighbour_second, preferred_element_type=jnp.float32)
    ).astype(jnp.bfloat16)
    grad_self = contract(layer_out, cotangent)
    grad_neighbour = contract(mean_second, cotangent)
    grad_self, grad_neighbour = lax.psum((grad_self, grad_neighbour), ("feat", "dom"))
    return (second_out, grad_self, grad_neighbour)


def solution(mesh):
    placed = (
        P("feat", "dom"),
        P("dom", None),
        P(),
        P(),
        P(("feat", "dom"), None),
        P(("feat", "dom"), None),
        P(),
        P(),
        P(("feat", "dom"), None),
    )
    return jax.shard_map(
        shards,
        mesh=mesh,
        in_specs=placed,
        out_specs=(P(("feat", "dom"), None), P(), P()),
        check_vma=False,
    )
```

```python
import jax
import jax.numpy as jnp
from jax import lax
from jax.experimental import pallas as pl
from jax.experimental.pallas import tpu as pltpu
from jax.sharding import PartitionSpec as P


def contract(left, right):
    return lax.dot_general(
        left, right, (((0,), (0,)), ((), ())), preferred_element_type=jnp.float32
    )


def gather_sum(table, index, block=512, unroll=8):
    fanout, count = index.shape
    rows, width = table.shape

    def kernel(index_ref, table_ref, out_ref):
        step = pl.program_id(0)

        def body(t, carry):
            base = step * block + t
            acc = table_ref[pl.ds(index_ref[base], 1), :]
            for k in range(1, fanout):
                acc = acc + table_ref[pl.ds(index_ref[k * count + base], 1), :]
            out_ref[pl.ds(t, 1), :] = acc
            return carry

        lax.fori_loop(0, block, body, 0, unroll=unroll)

    return pl.pallas_call(
        kernel,
        out_shape=jax.ShapeDtypeStruct((count, width), jnp.float32),
        grid_spec=pltpu.PrefetchScalarGridSpec(
            num_scalar_prefetch=1,
            grid=(count // block,),
            in_specs=[pl.BlockSpec((rows, width), lambda b, i: (0, 0))],
            out_specs=pl.BlockSpec((block, width), lambda b, i: (b, 0)),
        ),
    )(index.reshape(-1), table)


def shards(
    features,
    neighbours,
    self_first,
    neighbour_first,
    owners,
    offsets,
    self_second,
    neighbour_second,
    cotangent,
):
    columns_here = features.shape[0]
    targets_part = neighbours.shape[0]
    fanout_first = neighbours.shape[1]
    hidden_width = self_first.shape[1]
    feat_size = lax.axis_size("feat")
    share_rows = targets_part // feat_size
    cuts = [0, 3 * share_rows // 8, share_rows]
    weights = jnp.stack(
        [
            self_first.reshape(feat_size, columns_here, hidden_width),
            neighbour_first.reshape(feat_size, columns_here, hidden_width),
        ],
        axis=1,
    ).reshape(-1, hidden_width)
    table = features.astype(jnp.float32).T
    lists = neighbours.T.reshape(fanout_first, feat_size, share_rows)
    own_all = features[:, :targets_part].reshape(columns_here, feat_size, share_rows)
    seed_rows = cotangent.shape[0]
    fanout_second = offsets.shape[1]
    slot_owner = owners.reshape(seed_rows, fanout_second)
    layer_parts = []
    summed = None
    for c in range(len(cuts) - 1):
        first, piece_rows = cuts[c], cuts[c + 1] - cuts[c]
        rows = slice(first, first + piece_rows)
        mixed_rows = (
            gather_sum(table, lists[:, :, rows].reshape(fanout_first, -1)) / fanout_first
        ).astype(jnp.bfloat16)
        own_rows = jnp.transpose(own_all[:, :, rows], (1, 2, 0))
        both = jnp.stack(
            [own_rows, mixed_rows.reshape(feat_size, piece_rows, columns_here)], axis=2
        )
        arrived = lax.all_to_all(both, "feat", 0, 0, tiled=True)
        lhs = jnp.transpose(arrived, (1, 0, 2, 3)).reshape(piece_rows, -1)
        pre_first = jnp.dot(lhs, weights, preferred_element_type=jnp.float32)
        part_out = jnp.maximum(pre_first, 0.0).astype(jnp.bfloat16)
        layer_parts.append(part_out)
        segment = lax.all_gather(part_out, "dom", axis=0, tiled=True)
        inside = (offsets >= first) & (offsets < first + piece_rows)
        flat_rows = jnp.where(inside, slot_owner * piece_rows + offsets - first, -1)
        table_index = jnp.arange(segment.shape[0], dtype=jnp.int32)[None, :]
        counts = sum(
            (flat_rows[:, k : k + 1] == table_index).astype(jnp.bfloat16)
            for k in range(fanout_second)
        )
        counts = lax.optimization_barrier(counts)
        term = jnp.dot(counts, segment, preferred_element_type=jnp.float32)
        summed = term if summed is None else summed + term
    layer_out = jnp.concatenate(layer_parts, axis=0)
    mean_second = (summed / fanout_second).astype(jnp.bfloat16)
    second_out = (
        jnp.dot(layer_out, self_second, preferred_element_type=jnp.float32)
        + jnp.dot(mean_second, neighbour_second, preferred_element_type=jnp.float32)
    ).astype(jnp.bfloat16)
    grad_self = contract(layer_out, cotangent)
    grad_neighbour = contract(mean_second, cotangent)
    grad_self, grad_neighbour = lax.psum((grad_self, grad_neighbour), ("feat", "dom"))
    return (second_out, grad_self, grad_neighbour)


def solution(mesh):
    placed = (
        P("feat", "dom"),
        P("dom", None),
        P(),
        P(),
        P(("feat", "dom"), None),
        P(("feat", "dom"), None),
        P(),
        P(),
        P(("feat", "dom"), None),
    )
    return jax.shard_map(
        shards,
        mesh=mesh,
        in_specs=placed,
        out_specs=(P(("feat", "dom"), None), P(), P()),
        check_vma=False,
    )
```

```python
import jax
import jax.numpy as jnp
from jax import lax
from jax.experimental import pallas as pl
from jax.experimental.pallas import tpu as pltpu
from jax.sharding import PartitionSpec as P


def contract(left, right):
    return lax.dot_general(
        left, right, (((0,), (0,)), ((), ())), preferred_element_type=jnp.float32
    )


def gather_sum(table, index, block=512, unroll=8):
    fanout, count = index.shape
    rows, width = table.shape

    def kernel(index_ref, table_ref, out_ref):
        step = pl.program_id(0)

        def body(t, carry):
            base = step * block + t
            acc = table_ref[pl.ds(index_ref[base], 1), :]
            for k in range(1, fanout):
                acc = acc + table_ref[pl.ds(index_ref[k * count + base], 1), :]
            out_ref[pl.ds(t, 1), :] = acc
            return carry

        lax.fori_loop(0, block, body, 0, unroll=unroll)

    return pl.pallas_call(
        kernel,
        out_shape=jax.ShapeDtypeStruct((count, width), jnp.float32),
        grid_spec=pltpu.PrefetchScalarGridSpec(
            num_scalar_prefetch=1,
            grid=(count // block,),
            in_specs=[pl.BlockSpec((rows, width), lambda b, i: (0, 0))],
            out_specs=pl.BlockSpec((block, width), lambda b, i: (b, 0)),
        ),
    )(index.reshape(-1), table)


def shards(
    features,
    neighbours,
    self_first,
    neighbour_first,
    owners,
    offsets,
    self_second,
    neighbour_second,
    cotangent,
):
    columns_here = features.shape[0]
    targets_part = neighbours.shape[0]
    fanout_first = neighbours.shape[1]
    hidden_width = self_first.shape[1]
    feat_size = lax.axis_size("feat")
    share_rows = targets_part // feat_size
    cuts = [0, 3 * share_rows // 8, share_rows]
    weights = jnp.stack(
        [
            self_first.reshape(feat_size, columns_here, hidden_width),
            neighbour_first.reshape(feat_size, columns_here, hidden_width),
        ],
        axis=1,
    )
    here = lax.axis_index("feat")
    shifts = jnp.arange(feat_size, dtype=jnp.int32)
    weights = weights[(here - shifts) % feat_size].reshape(-1, hidden_width)
    sends = (here + shifts) % feat_size
    table = features.astype(jnp.float32).T
    lists = neighbours.T.reshape(fanout_first, feat_size, share_rows)
    own_all = features[:, :targets_part].reshape(columns_here, feat_size, share_rows)
    seed_rows = cotangent.shape[0]
    fanout_second = offsets.shape[1]
    slot_owner = owners.reshape(seed_rows, fanout_second)
    layer_parts = []
    summed = None
    for c in range(len(cuts) - 1):
        first, piece_rows = cuts[c], cuts[c + 1] - cuts[c]
        rows = slice(first, first + piece_rows)
        mixed_rows = (
            gather_sum(table, lists[:, :, rows].reshape(fanout_first, -1)) / fanout_first
        ).astype(jnp.bfloat16)
        own_rows = jnp.transpose(own_all[:, :, rows], (1, 2, 0))
        both = jnp.stack(
            [own_rows, mixed_rows.reshape(feat_size, piece_rows, columns_here)], axis=2
        )
        rolled = both[sends]
        arrived = jnp.stack(
            [rolled[0]]
            + [
                lax.ppermute(
                    rolled[j], "feat", [(i, (i + j) % feat_size) for i in range(feat_size)]
                )
                for j in range(1, feat_size)
            ]
        )
        lhs = jnp.transpose(arrived, (1, 0, 2, 3)).reshape(piece_rows, -1)
        pre_first = jnp.dot(lhs, weights, preferred_element_type=jnp.float32)
        part_out = jnp.maximum(pre_first, 0.0).astype(jnp.bfloat16)
        layer_parts.append(part_out)
        segment = lax.all_gather(part_out, "dom", axis=0, tiled=True)
        inside = (offsets >= first) & (offsets < first + piece_rows)
        flat_rows = jnp.where(inside, slot_owner * piece_rows + offsets - first, -1)
        table_index = jnp.arange(segment.shape[0], dtype=jnp.int32)[None, :]
        counts = sum(
            (flat_rows[:, k : k + 1] == table_index).astype(jnp.bfloat16)
            for k in range(fanout_second)
        )
        counts = lax.optimization_barrier(counts)
        term = jnp.dot(counts, segment, preferred_element_type=jnp.float32)
        summed = term if summed is None else summed + term
    layer_out = jnp.concatenate(layer_parts, axis=0)
    mean_second = (summed / fanout_second).astype(jnp.bfloat16)
    second_out = (
        jnp.dot(layer_out, self_second, preferred_element_type=jnp.float32)
        + jnp.dot(mean_second, neighbour_second, preferred_element_type=jnp.float32)
    ).astype(jnp.bfloat16)
    grad_self = contract(layer_out, cotangent)
    grad_neighbour = contract(mean_second, cotangent)
    grad_self, grad_neighbour = lax.psum((grad_self, grad_neighbour), ("feat", "dom"))
    return (second_out, grad_self, grad_neighbour)


def solution(mesh):
    placed = (
        P("feat", "dom"),
        P("dom", None),
        P(),
        P(),
        P(("feat", "dom"), None),
        P(("feat", "dom"), None),
        P(),
        P(),
        P(("feat", "dom"), None),
    )
    return jax.shard_map(
        shards,
        mesh=mesh,
        in_specs=placed,
        out_specs=(P(("feat", "dom"), None), P(), P()),
        check_vma=False,
    )
```

```python
import jax
import jax.numpy as jnp
from jax import lax
from jax.experimental import pallas as pl
from jax.experimental.pallas import tpu as pltpu
from jax.sharding import PartitionSpec as P


def contract(left, right):
    return lax.dot_general(
        left, right, (((0,), (0,)), ((), ())), preferred_element_type=jnp.float32
    )


def gather_sum(table, index, unroll=8):
    fanout, count = index.shape
    block = 512 if count % 512 == 0 else 256
    rows, width = table.shape

    def kernel(index_ref, table_ref, out_ref):
        step = pl.program_id(0)

        def body(t, carry):
            base = step * block + t
            acc = table_ref[pl.ds(index_ref[base], 1), :]
            for k in range(1, fanout):
                acc = acc + table_ref[pl.ds(index_ref[k * count + base], 1), :]
            out_ref[pl.ds(t, 1), :] = acc
            return carry

        lax.fori_loop(0, block, body, 0, unroll=unroll)

    return pl.pallas_call(
        kernel,
        out_shape=jax.ShapeDtypeStruct((count, width), jnp.float32),
        grid_spec=pltpu.PrefetchScalarGridSpec(
            num_scalar_prefetch=1,
            grid=(count // block,),
            in_specs=[pl.BlockSpec((rows, width), lambda b, i: (0, 0))],
            out_specs=pl.BlockSpec((block, width), lambda b, i: (b, 0)),
        ),
    )(index.reshape(-1), table)


def shards(
    features,
    neighbours,
    self_first,
    neighbour_first,
    owners,
    offsets,
    self_second,
    neighbour_second,
    cotangent,
):
    columns_here = features.shape[0]
    targets_part = neighbours.shape[0]
    fanout_first = neighbours.shape[1]
    hidden_width = self_first.shape[1]
    feat_size = lax.axis_size("feat")
    share_rows = targets_part // feat_size
    cuts = [0, 7 * share_rows // 16, share_rows]
    weights = jnp.stack(
        [
            self_first.reshape(feat_size, columns_here, hidden_width),
            neighbour_first.reshape(feat_size, columns_here, hidden_width),
        ],
        axis=1,
    ).reshape(-1, hidden_width)
    table = features.astype(jnp.float32).T
    lists = neighbours.T.reshape(fanout_first, feat_size, share_rows)
    own_all = features[:, :targets_part].reshape(columns_here, feat_size, share_rows)
    seed_rows = cotangent.shape[0]
    fanout_second = offsets.shape[1]
    slot_owner = owners.reshape(seed_rows, fanout_second)
    layer_parts = []
    summed = None
    for c in range(len(cuts) - 1):
        first, piece_rows = cuts[c], cuts[c + 1] - cuts[c]
        rows = slice(first, first + piece_rows)
        mixed_rows = (
            gather_sum(table, lists[:, :, rows].reshape(fanout_first, -1)) / fanout_first
        ).astype(jnp.bfloat16)
        own_rows = jnp.transpose(own_all[:, :, rows], (1, 2, 0))
        both = jnp.stack(
            [own_rows, mixed_rows.reshape(feat_size, piece_rows, columns_here)], axis=2
        )
        arrived = lax.all_to_all(both, "feat", 0, 0, tiled=True)
        lhs = jnp.transpose(arrived, (1, 0, 2, 3)).reshape(piece_rows, -1)
        pre_first = jnp.dot(lhs, weights, preferred_element_type=jnp.float32)
        part_out = jnp.maximum(pre_first, 0.0).astype(jnp.bfloat16)
        layer_parts.append(part_out)
        segment = lax.all_gather(part_out, "dom", axis=0, tiled=True)
        inside = (offsets >= first) & (offsets < first + piece_rows)
        flat_rows = jnp.where(inside, slot_owner * piece_rows + offsets - first, -1)
        table_index = jnp.arange(segment.shape[0], dtype=jnp.int32)[None, :]
        counts = sum(
            (flat_rows[:, k : k + 1] == table_index).astype(jnp.bfloat16)
            for k in range(fanout_second)
        )
        counts = lax.optimization_barrier(counts)
        term = jnp.dot(counts, segment, preferred_element_type=jnp.float32)
        summed = term if summed is None else summed + term
    layer_out = jnp.concatenate(layer_parts, axis=0)
    mean_second = (summed / fanout_second).astype(jnp.bfloat16)
    second_out = (
        jnp.dot(layer_out, self_second, preferred_element_type=jnp.float32)
        + jnp.dot(mean_second, neighbour_second, preferred_element_type=jnp.float32)
    ).astype(jnp.bfloat16)
    grad_self = contract(layer_out, cotangent)
    grad_neighbour = contract(mean_second, cotangent)
    grad_self, grad_neighbour = lax.psum((grad_self, grad_neighbour), ("feat", "dom"))
    return (second_out, grad_self, grad_neighbour)


def solution(mesh):
    placed = (
        P("feat", "dom"),
        P("dom", None),
        P(),
        P(),
        P(("feat", "dom"), None),
        P(("feat", "dom"), None),
        P(),
        P(),
        P(("feat", "dom"), None),
    )
    return jax.shard_map(
        shards,
        mesh=mesh,
        in_specs=placed,
        out_specs=(P(("feat", "dom"), None), P(), P()),
        check_vma=False,
    )
```

```python
import jax
import jax.numpy as jnp
from jax import lax
from jax.experimental import pallas as pl
from jax.experimental.pallas import tpu as pltpu
from jax.sharding import PartitionSpec as P


def contract(left, right):
    return lax.dot_general(
        left, right, (((0,), (0,)), ((), ())), preferred_element_type=jnp.float32
    )


def gather_sum(table, index, block=512, unroll=16):
    fanout, count = index.shape
    rows, width = table.shape

    def kernel(index_ref, table_ref, out_ref):
        step = pl.program_id(0)

        def body(t, carry):
            base = step * block + t
            acc = table_ref[pl.ds(index_ref[base], 1), :]
            for k in range(1, fanout):
                acc = acc + table_ref[pl.ds(index_ref[k * count + base], 1), :]
            out_ref[pl.ds(t, 1), :] = acc
            return carry

        lax.fori_loop(0, block, body, 0, unroll=unroll)

    return pl.pallas_call(
        kernel,
        out_shape=jax.ShapeDtypeStruct((count, width), jnp.float32),
        grid_spec=pltpu.PrefetchScalarGridSpec(
            num_scalar_prefetch=1,
            grid=(count // block,),
            in_specs=[pl.BlockSpec((rows, width), lambda b, i: (0, 0))],
            out_specs=pl.BlockSpec((block, width), lambda b, i: (b, 0)),
        ),
    )(index.reshape(-1), table)


def shards(
    features,
    neighbours,
    self_first,
    neighbour_first,
    owners,
    offsets,
    self_second,
    neighbour_second,
    cotangent,
):
    columns_here = features.shape[0]
    targets_part = neighbours.shape[0]
    fanout_first = neighbours.shape[1]
    hidden_width = self_first.shape[1]
    feat_size = lax.axis_size("feat")
    share_rows = targets_part // feat_size
    cuts = [0, 3 * share_rows // 8, share_rows]
    weights = jnp.stack(
        [
            self_first.reshape(feat_size, columns_here, hidden_width),
            neighbour_first.reshape(feat_size, columns_here, hidden_width),
        ],
        axis=1,
    ).reshape(-1, hidden_width)
    table = features.astype(jnp.float32).T
    lists = neighbours.T.reshape(fanout_first, feat_size, share_rows)
    own_all = features[:, :targets_part].reshape(columns_here, feat_size, share_rows)
    seed_rows = cotangent.shape[0]
    fanout_second = offsets.shape[1]
    slot_owner = owners.reshape(seed_rows, fanout_second)
    layer_parts = []
    summed = None
    for c in range(len(cuts) - 1):
        first, piece_rows = cuts[c], cuts[c + 1] - cuts[c]
        rows = slice(first, first + piece_rows)
        mixed_rows = (
            gather_sum(table, lists[:, :, rows].reshape(fanout_first, -1)) / fanout_first
        ).astype(jnp.bfloat16)
        own_rows = jnp.transpose(own_all[:, :, rows], (1, 2, 0))
        both = jnp.stack(
            [own_rows, mixed_rows.reshape(feat_size, piece_rows, columns_here)], axis=2
        )
        arrived = lax.all_to_all(both, "feat", 0, 0, tiled=True)
        lhs = jnp.transpose(arrived, (1, 0, 2, 3)).reshape(piece_rows, -1)
        pre_first = jnp.dot(lhs, weights, preferred_element_type=jnp.float32)
        part_out = jnp.maximum(pre_first, 0.0).astype(jnp.bfloat16)
        layer_parts.append(part_out)
        segment = lax.all_gather(part_out, "dom", axis=0, tiled=True)
        inside = (offsets >= first) & (offsets < first + piece_rows)
        flat_rows = jnp.where(inside, slot_owner * piece_rows + offsets - first, -1)
        table_index = jnp.arange(segment.shape[0], dtype=jnp.int32)[None, :]
        counts = sum(
            (flat_rows[:, k : k + 1] == table_index).astype(jnp.bfloat16)
            for k in range(fanout_second)
        )
        counts = lax.optimization_barrier(counts)
        term = jnp.dot(counts, segment, preferred_element_type=jnp.float32)
        summed = term if summed is None else summed + term
    layer_out = jnp.concatenate(layer_parts, axis=0)
    mean_second = (summed / fanout_second).astype(jnp.bfloat16)
    second_out = (
        jnp.dot(layer_out, self_second, preferred_element_type=jnp.float32)
        + jnp.dot(mean_second, neighbour_second, preferred_element_type=jnp.float32)
    ).astype(jnp.bfloat16)
    grad_self = contract(layer_out, cotangent)
    grad_neighbour = contract(mean_second, cotangent)
    grad_self, grad_neighbour = lax.psum((grad_self, grad_neighbour), ("feat", "dom"))
    return (second_out, grad_self, grad_neighbour)


def solution(mesh):
    placed = (
        P("feat", "dom"),
        P("dom", None),
        P(),
        P(),
        P(("feat", "dom"), None),
        P(("feat", "dom"), None),
        P(),
        P(),
        P(("feat", "dom"), None),
    )
    return jax.shard_map(
        shards,
        mesh=mesh,
        in_specs=placed,
        out_specs=(P(("feat", "dom"), None), P(), P()),
        check_vma=False,
    )
```

```python
import jax
import jax.numpy as jnp
from jax import lax
from jax.experimental import pallas as pl
from jax.experimental.pallas import tpu as pltpu
from jax.sharding import PartitionSpec as P


def contract(left, right):
    return lax.dot_general(
        left, right, (((0,), (0,)), ((), ())), preferred_element_type=jnp.float32
    )


def gather_sum(table, index, block=512, unroll=32):
    fanout, count = index.shape
    rows, width = table.shape

    def kernel(index_ref, table_ref, out_ref):
        step = pl.program_id(0)

        def body(t, carry):
            base = step * block + t
            acc = table_ref[pl.ds(index_ref[base], 1), :]
            for k in range(1, fanout):
                acc = acc + table_ref[pl.ds(index_ref[k * count + base], 1), :]
            out_ref[pl.ds(t, 1), :] = acc
            return carry

        lax.fori_loop(0, block, body, 0, unroll=unroll)

    return pl.pallas_call(
        kernel,
        out_shape=jax.ShapeDtypeStruct((count, width), jnp.float32),
        grid_spec=pltpu.PrefetchScalarGridSpec(
            num_scalar_prefetch=1,
            grid=(count // block,),
            in_specs=[pl.BlockSpec((rows, width), lambda b, i: (0, 0))],
            out_specs=pl.BlockSpec((block, width), lambda b, i: (b, 0)),
        ),
    )(index.reshape(-1), table)


def shards(
    features,
    neighbours,
    self_first,
    neighbour_first,
    owners,
    offsets,
    self_second,
    neighbour_second,
    cotangent,
):
    columns_here = features.shape[0]
    targets_part = neighbours.shape[0]
    fanout_first = neighbours.shape[1]
    hidden_width = self_first.shape[1]
    feat_size = lax.axis_size("feat")
    share_rows = targets_part // feat_size
    cuts = [0, 3 * share_rows // 8, share_rows]
    weights = jnp.stack(
        [
            self_first.reshape(feat_size, columns_here, hidden_width),
            neighbour_first.reshape(feat_size, columns_here, hidden_width),
        ],
        axis=1,
    ).reshape(-1, hidden_width)
    table = features.astype(jnp.float32).T
    lists = neighbours.T.reshape(fanout_first, feat_size, share_rows)
    own_all = features[:, :targets_part].reshape(columns_here, feat_size, share_rows)
    seed_rows = cotangent.shape[0]
    fanout_second = offsets.shape[1]
    slot_owner = owners.reshape(seed_rows, fanout_second)
    layer_parts = []
    summed = None
    for c in range(len(cuts) - 1):
        first, piece_rows = cuts[c], cuts[c + 1] - cuts[c]
        rows = slice(first, first + piece_rows)
        mixed_rows = (
            gather_sum(table, lists[:, :, rows].reshape(fanout_first, -1)) / fanout_first
        ).astype(jnp.bfloat16)
        own_rows = jnp.transpose(own_all[:, :, rows], (1, 2, 0))
        both = jnp.stack(
            [own_rows, mixed_rows.reshape(feat_size, piece_rows, columns_here)], axis=2
        )
        arrived = lax.all_to_all(both, "feat", 0, 0, tiled=True)
        lhs = jnp.transpose(arrived, (1, 0, 2, 3)).reshape(piece_rows, -1)
        pre_first = jnp.dot(lhs, weights, preferred_element_type=jnp.float32)
        part_out = jnp.maximum(pre_first, 0.0).astype(jnp.bfloat16)
        layer_parts.append(part_out)
        segment = lax.all_gather(part_out, "dom", axis=0, tiled=True)
        inside = (offsets >= first) & (offsets < first + piece_rows)
        flat_rows = jnp.where(inside, slot_owner * piece_rows + offsets - first, -1)
        table_index = jnp.arange(segment.shape[0], dtype=jnp.int32)[None, :]
        counts = sum(
            (flat_rows[:, k : k + 1] == table_index).astype(jnp.bfloat16)
            for k in range(fanout_second)
        )
        counts = lax.optimization_barrier(counts)
        term = jnp.dot(counts, segment, preferred_element_type=jnp.float32)
        summed = term if summed is None else summed + term
    layer_out = jnp.concatenate(layer_parts, axis=0)
    mean_second = (summed / fanout_second).astype(jnp.bfloat16)
    second_out = (
        jnp.dot(layer_out, self_second, preferred_element_type=jnp.float32)
        + jnp.dot(mean_second, neighbour_second, preferred_element_type=jnp.float32)
    ).astype(jnp.bfloat16)
    grad_self = contract(layer_out, cotangent)
    grad_neighbour = contract(mean_second, cotangent)
    grad_self, grad_neighbour = lax.psum((grad_self, grad_neighbour), ("feat", "dom"))
    return (second_out, grad_self, grad_neighbour)


def solution(mesh):
    placed = (
        P("feat", "dom"),
        P("dom", None),
        P(),
        P(),
        P(("feat", "dom"), None),
        P(("feat", "dom"), None),
        P(),
        P(),
        P(("feat", "dom"), None),
    )
    return jax.shard_map(
        shards,
        mesh=mesh,
        in_specs=placed,
        out_specs=(P(("feat", "dom"), None), P(), P()),
        check_vma=False,
    )
```

```python
import jax
import jax.numpy as jnp
from jax import lax
from jax.experimental import pallas as pl
from jax.experimental.pallas import tpu as pltpu
from jax.sharding import PartitionSpec as P


def contract(left, right):
    return lax.dot_general(
        left, right, (((0,), (0,)), ((), ())), preferred_element_type=jnp.float32
    )


def gather_sum(table, index, block=512, unroll=64):
    fanout, count = index.shape
    rows, width = table.shape

    def kernel(index_ref, table_ref, out_ref):
        step = pl.program_id(0)

        def body(t, carry):
            base = step * block + t
            acc = table_ref[pl.ds(index_ref[base], 1), :]
            for k in range(1, fanout):
                acc = acc + table_ref[pl.ds(index_ref[k * count + base], 1), :]
            out_ref[pl.ds(t, 1), :] = acc
            return carry

        lax.fori_loop(0, block, body, 0, unroll=unroll)

    return pl.pallas_call(
        kernel,
        out_shape=jax.ShapeDtypeStruct((count, width), jnp.float32),
        grid_spec=pltpu.PrefetchScalarGridSpec(
            num_scalar_prefetch=1,
            grid=(count // block,),
            in_specs=[pl.BlockSpec((rows, width), lambda b, i: (0, 0))],
            out_specs=pl.BlockSpec((block, width), lambda b, i: (b, 0)),
        ),
    )(index.reshape(-1), table)


def shards(
    features,
    neighbours,
    self_first,
    neighbour_first,
    owners,
    offsets,
    self_second,
    neighbour_second,
    cotangent,
):
    columns_here = features.shape[0]
    targets_part = neighbours.shape[0]
    fanout_first = neighbours.shape[1]
    hidden_width = self_first.shape[1]
    feat_size = lax.axis_size("feat")
    share_rows = targets_part // feat_size
    cuts = [0, 3 * share_rows // 8, share_rows]
    weights = jnp.stack(
        [
            self_first.reshape(feat_size, columns_here, hidden_width),
            neighbour_first.reshape(feat_size, columns_here, hidden_width),
        ],
        axis=1,
    ).reshape(-1, hidden_width)
    table = features.astype(jnp.float32).T
    lists = neighbours.T.reshape(fanout_first, feat_size, share_rows)
    own_all = features[:, :targets_part].reshape(columns_here, feat_size, share_rows)
    seed_rows = cotangent.shape[0]
    fanout_second = offsets.shape[1]
    slot_owner = owners.reshape(seed_rows, fanout_second)
    layer_parts = []
    summed = None
    for c in range(len(cuts) - 1):
        first, piece_rows = cuts[c], cuts[c + 1] - cuts[c]
        rows = slice(first, first + piece_rows)
        mixed_rows = (
            gather_sum(table, lists[:, :, rows].reshape(fanout_first, -1)) / fanout_first
        ).astype(jnp.bfloat16)
        own_rows = jnp.transpose(own_all[:, :, rows], (1, 2, 0))
        both = jnp.stack(
            [own_rows, mixed_rows.reshape(feat_size, piece_rows, columns_here)], axis=2
        )
        arrived = lax.all_to_all(both, "feat", 0, 0, tiled=True)
        lhs = jnp.transpose(arrived, (1, 0, 2, 3)).reshape(piece_rows, -1)
        pre_first = jnp.dot(lhs, weights, preferred_element_type=jnp.float32)
        part_out = jnp.maximum(pre_first, 0.0).astype(jnp.bfloat16)
        layer_parts.append(part_out)
        segment = lax.all_gather(part_out, "dom", axis=0, tiled=True)
        inside = (offsets >= first) & (offsets < first + piece_rows)
        flat_rows = jnp.where(inside, slot_owner * piece_rows + offsets - first, -1)
        table_index = jnp.arange(segment.shape[0], dtype=jnp.int32)[None, :]
        counts = sum(
            (flat_rows[:, k : k + 1] == table_index).astype(jnp.bfloat16)
            for k in range(fanout_second)
        )
        counts = lax.optimization_barrier(counts)
        term = jnp.dot(counts, segment, preferred_element_type=jnp.float32)
        summed = term if summed is None else summed + term
    layer_out = jnp.concatenate(layer_parts, axis=0)
    mean_second = (summed / fanout_second).astype(jnp.bfloat16)
    second_out = (
        jnp.dot(layer_out, self_second, preferred_element_type=jnp.float32)
        + jnp.dot(mean_second, neighbour_second, preferred_element_type=jnp.float32)
    ).astype(jnp.bfloat16)
    grad_self = contract(layer_out, cotangent)
    grad_neighbour = contract(mean_second, cotangent)
    grad_self, grad_neighbour = lax.psum((grad_self, grad_neighbour), ("feat", "dom"))
    return (second_out, grad_self, grad_neighbour)


def solution(mesh):
    placed = (
        P("feat", "dom"),
        P("dom", None),
        P(),
        P(),
        P(("feat", "dom"), None),
        P(("feat", "dom"), None),
        P(),
        P(),
        P(("feat", "dom"), None),
    )
    return jax.shard_map(
        shards,
        mesh=mesh,
        in_specs=placed,
        out_specs=(P(("feat", "dom"), None), P(), P()),
        check_vma=False,
    )
```
